128 devices in a mesh: ang: 4 (over y), pix: 32 (over x, z, core).
Axes of the slice: x: 4, y: 4, z: 4, core: 2. Of those that a mesh axis runs over, the one named last changes fastest.
Arguments:
- flats: float32 [256, 256, 4096], P(None, 'pix', 'ang'), may hold values from -60 to 60
- projections: float32 [128, 256, 4096], P('ang', None, 'pix'), may hold values from -60 to 60
- start_basis: float32 [256, 48], replicated, may hold values from -0.375 to 0.375
Outputs:
- corrected: float32 [128, 256, 4096], P('ang', None, 'pix')
The draws below stay inside these ranges and needn't reach their ends.
All inputs are finite; a program needn't handle non-finite values.
Results may differ from the reference program's by a relative error of at most 0.0001.
Values sent between devices are 32-bit elements; how exact they have to be, the bound alone decides.
No kernel may reach another device: no remote copies, remote signals or barrier semaphores. Data moves between devices by JAX's collectives and lax.ppermute only.
A program may use at most 128 MiB of HBM per device.

```python
import jax
import jax.numpy as jnp
from jax import lax

NF = 256
NEIG = 48
SUBSPACE = 2
ROWS = 256
COLS = 4096
NPROJ = 128


mode_count = 64


def base_field(key):
    key_base = jax.random.fold_in(key, 101)
    rows = jnp.arange(ROWS, dtype=jnp.float32) / ROWS
    ramp = 0.5 + rows
    rough = jnp.exp(jax.random.uniform(key_base, (ROWS, COLS), jnp.float32, -0.4, 0.4))
    return ramp[:, None] * rough


def shaped(key, amps):
    key_modes = jax.random.fold_in(key, 202)

    def add_mode(index, total):
        field = 0.12 * jax.random.truncated_normal(jax.random.fold_in(key_modes, index), -3.0, 3.0, (ROWS, COLS), jnp.float32)
        decay = lax.rsqrt(1.0 + index.astype(jnp.float32))
        column = lax.dynamic_index_in_dim(amps, index, 1, keepdims=False) * decay
        return total + column[:, None, None] * field[None]
    start = jnp.ones((amps.shape[0], ROWS, COLS), jnp.float32)
    total = lax.fori_loop(0, mode_count, add_mode, start)
    return base_field(key)[None] * total


def draw_flats(key, part):
    amps = jax.random.truncated_normal(jax.random.fold_in(key, 303), -3.0, 3.0, (NF, mode_count), jnp.float32)
    key_noise = jax.random.fold_in(key, 404)
    noise = 0.005 * jax.random.truncated_normal(key_noise, -4.0, 4.0, (NF, ROWS, COLS), jnp.float32)
    return shaped(key, amps) + noise


def draw_projections(key, part):
    amps = jax.random.truncated_normal(jax.random.fold_in(key, 505), -3.0, 3.0, (NPROJ, mode_count), jnp.float32)
    sample = jax.random.uniform(jax.random.fold_in(key, 606), (NPROJ, ROWS, COLS), jnp.float32, 0.3, 1.0)
    key_noise = jax.random.fold_in(key, 707)
    noise = 0.02 * jax.random.truncated_normal(key_noise, -4.0, 4.0, (NPROJ, ROWS, COLS), jnp.float32)
    return shaped(key, amps) * sample + noise


def centred(key, shape, spread, limit, held_as=jnp.bfloat16):
    array = jax.random.normal(key, shape, jnp.float32) * spread
    return jnp.minimum(jnp.maximum(array, -limit), limit).astype(held_as)


def setup_inputs(seed: int = 0) -> dict:
    splits = jax.random.split(jax.random.key(seed), 4)
    flats = draw_flats(jax.random.fold_in(splits[3], 71), 0)
    projections = draw_projections(jax.random.fold_in(splits[3], 71), 0)
    start_basis = centred(splits[2], (NF, NEIG), NF ** -0.5, 0.375, jnp.float32)
    return {"flats": flats, "projections": projections, "start_basis": start_basis}


floor_value = 0.2

def factor_lower(matrix):
    order = matrix.shape[0]
    places = jnp.arange(order)

    def add_column(index, lower):
        pick = (places == index).astype(matrix.dtype)
        before = (places < index).astype(matrix.dtype)
        row_now = jnp.dot(pick, lower, precision=lax.Precision.HIGHEST) * before
        column = jnp.dot(matrix, pick, precision=lax.Precision.HIGHEST)
        pivot = jnp.sqrt(jnp.sum(column * pick) - jnp.sum(row_now * row_now))
        below = (column - jnp.dot(lower, row_now, precision=lax.Precision.HIGHEST)) / pivot
        fresh = jnp.where(places > index, below, jnp.zeros_like(below)) + pick * pivot
        return lower + fresh[:, None] * pick[None, :]
    return lax.fori_loop(0, order, add_column, jnp.zeros_like(matrix))

def solve_lower(lower, target):
    order = lower.shape[0]
    places = jnp.arange(order)

    def forward(index, solved):
        pick = (places == index).astype(lower.dtype)
        row_now = jnp.dot(pick, lower, precision=lax.Precision.HIGHEST)
        pivot = jnp.sum(row_now * pick)
        row_off = row_now * (places < index).astype(lower.dtype)
        value = (jnp.dot(pick, target, precision=lax.Precision.HIGHEST) - jnp.dot(row_off, solved, precision=lax.Precision.HIGHEST)) / pivot
        return solved + pick[:, None] * value[None, :]
    return lax.fori_loop(0, order, forward, jnp.zeros_like(target))

def solve_upper(lower, target):
    order = lower.shape[0]
    places = jnp.arange(order)

    def backward(turn, solved):
        index = order - 1 - turn
        pick = (places == index).astype(lower.dtype)
        row_now = jnp.dot(lower, pick, precision=lax.Precision.HIGHEST)
        pivot = jnp.sum(row_now * pick)
        row_off = row_now * (places > index).astype(lower.dtype)
        value = (jnp.dot(pick, target, precision=lax.Precision.HIGHEST) - jnp.dot(row_off, solved, precision=lax.Precision.HIGHEST)) / pivot
        return solved + pick[:, None] * value[None, :]
    return lax.fori_loop(0, order, backward, jnp.zeros_like(target))

def orthonormal(grown):
    correlation = jnp.dot(grown.T, grown, precision=lax.Precision.HIGHEST)
    lower = factor_lower(correlation)
    return solve_lower(lower, grown.T).T

def solve_normal(normal, fit_rhs):
    factor = factor_lower(normal)
    inner = solve_lower(factor, fit_rhs.T)
    return solve_upper(factor, inner).T

def reference(flats, projections, start_basis):
    npix = flats.shape[1] * flats.shape[2]
    mean_flat = lax.optimization_barrier(jnp.mean(flats, axis=0))
    centered = (flats - mean_flat).reshape(flats.shape[0], -1)
    gram = jnp.dot(centered, centered.T, precision=lax.Precision.HIGHEST) / npix
    basis = start_basis
    for turn in range(SUBSPACE):
        basis = orthonormal(jnp.dot(gram, basis, precision=lax.Precision.HIGHEST))
    eigen_flats = jnp.dot(basis.T, centered, precision=lax.Precision.HIGHEST)
    normal = jnp.dot(basis.T, jnp.dot(gram, basis, precision=lax.Precision.HIGHEST), precision=lax.Precision.HIGHEST)
    flat_row = mean_flat.reshape(1, -1)
    frames = projections.reshape(projections.shape[0], -1)
    fit_rhs = jnp.dot(frames - flat_row, eigen_flats.T, precision=lax.Precision.HIGHEST) / npix
    weights = solve_normal(normal, fit_rhs)
    estimate = flat_row + jnp.dot(weights, eigen_flats, precision=lax.Precision.HIGHEST)
    corrected = frames / jnp.maximum(estimate, floor_value)
    return corrected.reshape(projections.shape)
```

```python
import jax
import jax.numpy as jnp
from jax import lax
from jax.sharding import PartitionSpec as P

SUBSPACE = 2


floor_value = 0.2


def orthonormal(grown):
    correlation = jnp.dot(grown.T, grown, precision=lax.Precision.HIGHEST)
    lower = jnp.linalg.cholesky(correlation)
    return jax.scipy.linalg.solve_triangular(lower, grown.T, lower=True).T


def solve_normal(normal, fit_rhs):
    factor = jnp.linalg.cholesky(normal)
    return jax.scipy.linalg.cho_solve((factor, True), fit_rhs.T).T


def sum_by_exchange(rows, axes, count):
    total, width = rows.shape
    pieces = lax.all_to_all(rows.reshape(count, total // count, width), axes, 0, 0, tiled=True)
    block = jnp.sum(pieces, axis=0)
    spread = jnp.broadcast_to(block[None], (count,) + block.shape)
    gathered = lax.all_to_all(spread, axes, 0, 0, tiled=True)
    return gathered.reshape(total, width)


def shards(flats, projections, start_basis):
    frames_here, rows_dev, cols_dev = flats.shape
    ang_count = lax.axis_size("ang")
    pix_count = lax.axis_size("pix")
    npix = rows_dev * cols_dev * ang_count * pix_count
    angle_count, rows_all, cols_here = projections.shape

    tiles_in = projections.reshape(angle_count, pix_count, rows_dev, cols_here).transpose(1, 0, 2, 3)
    tiles = lax.all_to_all(tiles_in, "pix", 0, 0, tiled=True)

    mean_flat = jnp.mean(flats, axis=0)
    centered = (flats - mean_flat).reshape(frames_here, -1)
    local_gram = jnp.dot(centered, centered.T, precision=lax.Precision.HIGHEST)
    device_count = ang_count * pix_count
    gram_rows = local_gram.reshape(device_count, -1)
    gram = sum_by_exchange(gram_rows, ("ang", "pix"), device_count).reshape(frames_here, frames_here) / npix
    basis = start_basis
    for turn in range(SUBSPACE):
        basis = orthonormal(jnp.dot(gram, basis, precision=lax.Precision.HIGHEST))
    eigen_flats = jnp.dot(basis.T, centered, precision=lax.Precision.HIGHEST)
    normal = jnp.dot(
        basis.T,
        jnp.dot(gram, basis, precision=lax.Precision.HIGHEST),
        precision=lax.Precision.HIGHEST,
    )
    eigen_count = eigen_flats.shape[0]
    eigen_rows = lax.all_gather(
        eigen_flats.reshape(eigen_count, rows_dev, cols_dev), "ang", axis=2, tiled=True
    )
    mean_rows = lax.all_gather(mean_flat, "ang", axis=1, tiled=True)
    eigen_blk = eigen_rows.reshape(eigen_count, rows_dev, pix_count, cols_here)
    mean_blk = mean_rows.reshape(rows_dev, pix_count, cols_here)
    centred_frames = tiles - mean_blk.transpose(1, 0, 2)[:, None]
    partial_value = jnp.einsum(
        "pjrc,krpc->jk", centred_frames, eigen_blk, precision=lax.Precision.HIGHEST
    )
    fit_rhs = sum_by_exchange(partial_value, "pix", pix_count) / npix
    weights = solve_normal(normal, fit_rhs)
    estimate = mean_blk.transpose(1, 0, 2)[:, None] + jnp.einsum(
        "jk,krpc->pjrc", weights, eigen_blk, precision=lax.Precision.HIGHEST
    )
    tiles_out = tiles / jnp.maximum(estimate, floor_value)
    back = lax.all_to_all(tiles_out, "pix", 0, 0, tiled=True)
    result = back.transpose(1, 0, 2, 3).reshape(angle_count, rows_all, cols_here)
    return result


def solution(mesh):
    in_specs = (P(None, "pix", "ang"), P("ang", None, "pix"), P())
    out_specs = P("ang", None, "pix")
    return jax.shard_map(shards, mesh=mesh, in_specs=in_specs, out_specs=out_specs, check_vma=False)
```

```python
import jax
import jax.numpy as jnp
from jax import lax
from jax.sharding import PartitionSpec as P

SUBSPACE = 2


floor_value = 0.2


def orthonormal(grown):
    correlation = jnp.dot(grown.T, grown, precision=lax.Precision.HIGHEST)
    lower = jnp.linalg.cholesky(correlation)
    return jax.scipy.linalg.solve_triangular(lower, grown.T, lower=True).T


def solve_normal(normal, fit_rhs):
    factor = jnp.linalg.cholesky(normal)
    return jax.scipy.linalg.cho_solve((factor, True), fit_rhs.T).T


def sum_by_exchange(rows, axes, count):
    total, width = rows.shape
    pieces = lax.all_to_all(rows.reshape(count, total // count, width), axes, 0, 0, tiled=True)
    block = jnp.sum(pieces, axis=0)
    spread = jnp.broadcast_to(block[None], (count,) + block.shape)
    gathered = lax.all_to_all(spread, axes, 0, 0, tiled=True)
    return gathered.reshape(total, width)


def shards(flats, projections, start_basis):
    frames_here, rows_dev, cols_dev = flats.shape
    ang_count = lax.axis_size("ang")
    pix_count = lax.axis_size("pix")
    device_count = ang_count * pix_count
    npix = rows_dev * cols_dev * device_count
    angle_count, rows_all, cols_here = projections.shape
    sub_blocks = cols_dev // cols_here

    tiles_in = projections.reshape(angle_count, pix_count, rows_dev, cols_here).transpose(1, 0, 2, 3)
    by_rows = lax.all_to_all(tiles_in, "pix", 0, 0, tiled=True)
    by_groups = by_rows.reshape(ang_count, sub_blocks, angle_count, rows_dev, cols_here)
    by_pixels = lax.all_to_all(by_groups, "ang", 0, 0, tiled=True)
    frames = by_pixels.transpose(0, 2, 3, 1, 4).reshape(ang_count * angle_count, rows_dev * cols_dev)

    mean_flat = jnp.mean(flats, axis=0)
    centered = (flats - mean_flat).reshape(frames_here, -1)
    local_gram = jnp.dot(centered, centered.T, precision=lax.Precision.HIGHEST)
    gram_rows = local_gram.reshape(device_count, -1)
    gram = sum_by_exchange(gram_rows, ("ang", "pix"), device_count).reshape(frames_here, frames_here) / npix
    basis = start_basis
    for turn in range(SUBSPACE):
        basis = orthonormal(jnp.dot(gram, basis, precision=lax.Precision.HIGHEST))
    eigen_flats = jnp.dot(basis.T, centered, precision=lax.Precision.HIGHEST)
    normal = jnp.dot(
        basis.T,
        jnp.dot(gram, basis, precision=lax.Precision.HIGHEST),
        precision=lax.Precision.HIGHEST,
    )
    flat_row = mean_flat.reshape(1, -1)
    partial_value = jnp.dot(frames - flat_row, eigen_flats.T, precision=lax.Precision.HIGHEST)
    fit_rhs = sum_by_exchange(partial_value, ("ang", "pix"), device_count) / npix
    weights = solve_normal(normal, fit_rhs)
    estimate = flat_row + jnp.dot(weights, eigen_flats, precision=lax.Precision.HIGHEST)
    corrected = frames / jnp.maximum(estimate, floor_value)

    out_groups = corrected.reshape(ang_count, angle_count, rows_dev, sub_blocks, cols_here).transpose(0, 3, 1, 2, 4)
    by_cols = lax.all_to_all(out_groups, "ang", 0, 0, tiled=True)
    out_blocks = by_cols.reshape(pix_count, angle_count, rows_dev, cols_here)
    back = lax.all_to_all(out_blocks, "pix", 0, 0, tiled=True)
    return back.transpose(1, 0, 2, 3).reshape(angle_count, rows_all, cols_here)


def solution(mesh):
    in_specs = (P(None, "pix", "ang"), P("ang", None, "pix"), P())
    out_specs = P("ang", None, "pix")
    return jax.shard_map(shards, mesh=mesh, in_specs=in_specs, out_specs=out_specs, check_vma=False)
```

```python
import jax
import jax.numpy as jnp
from jax import lax
from jax.sharding import PartitionSpec as P
from jax.experimental import pallas as pl

SUBSPACE = 2


floor_value = 0.2


def orthonormal(grown):
    correlation = jnp.dot(grown.T, grown, precision=lax.Precision.HIGHEST)
    lower = jnp.linalg.cholesky(correlation)
    return jax.scipy.linalg.solve_triangular(lower, grown.T, lower=True).T


def solve_normal(normal, fit_rhs):
    factor = jnp.linalg.cholesky(normal)
    return jax.scipy.linalg.cho_solve((factor, True), fit_rhs.T).T


def sum_by_exchange(rows, axes, count):
    total, width = rows.shape
    pieces = lax.all_to_all(rows.reshape(count, total // count, width), axes, 0, 0, tiled=True)
    block = jnp.sum(pieces, axis=0)
    spread = jnp.broadcast_to(block[None], (count,) + block.shape)
    gathered = lax.all_to_all(spread, axes, 0, 0, tiled=True)
    return gathered.reshape(total, width)


def _project_kernel(lhs_ref, rhs_ref, out_ref):
    lhs = lhs_ref[...]
    for row in range(rhs_ref.shape[1]):
        out_ref[:, row, :] = jnp.dot(
            lhs, rhs_ref[:, row, :], precision=lax.Precision.HIGHEST,
            preferred_element_type=jnp.float32,
        )


def project_rows(lhs, rhs):
    m, k = lhs.shape
    _, rows, width = rhs.shape
    return pl.pallas_call(
        _project_kernel,
        grid=(1,),
        in_specs=[
            pl.BlockSpec((m, k), lambda r: (0, 0)),
            pl.BlockSpec((k, rows, width), lambda r: (0, 0, 0)),
        ],
        out_specs=pl.BlockSpec((m, rows, width), lambda r: (0, 0, 0)),
        out_shape=jax.ShapeDtypeStruct((m, rows, width), jnp.float32),
    )(lhs, rhs)


def shards(flats, projections, start_basis):
    frames_here, rows_dev, cols_dev = flats.shape
    ang_count = lax.axis_size("ang")
    pix_count = lax.axis_size("pix")
    npix = rows_dev * cols_dev * ang_count * pix_count
    angle_count, rows_all, cols_here = projections.shape

    tiles_in = projections.reshape(angle_count, pix_count, rows_dev, cols_here).transpose(1, 0, 2, 3)
    tiles = lax.all_to_all(tiles_in, "pix", 0, 0, tiled=True)

    mean_flat = jnp.mean(flats, axis=0)
    centered_rows = flats - mean_flat
    centered = centered_rows.reshape(frames_here, -1)
    local_gram = jnp.dot(centered, centered.T, precision=lax.Precision.HIGHEST)
    device_count = ang_count * pix_count
    gram_rows = local_gram.reshape(device_count, -1)
    gram = sum_by_exchange(gram_rows, ("ang", "pix"), device_count).reshape(frames_here, frames_here) / npix
    basis = start_basis
    for turn in range(SUBSPACE):
        basis = orthonormal(jnp.dot(gram, basis, precision=lax.Precision.HIGHEST))
    eigen_3d = project_rows(basis.T, centered_rows)
    eigen_flats = eigen_3d.reshape(basis.shape[1], -1)
    normal = jnp.dot(
        basis.T,
        jnp.dot(gram, basis, precision=lax.Precision.HIGHEST),
        precision=lax.Precision.HIGHEST,
    )
    eigen_count = eigen_flats.shape[0]
    eigen_rows = lax.all_gather(
        eigen_3d, "ang", axis=2, tiled=True
    )
    mean_rows = lax.all_gather(mean_flat, "ang", axis=1, tiled=True)
    eigen_blk = eigen_rows.reshape(eigen_count, rows_dev, pix_count, cols_here)
    mean_blk = mean_rows.reshape(rows_dev, pix_count, cols_here)
    centred_frames = tiles - mean_blk.transpose(1, 0, 2)[:, None]
    partial_value = jnp.einsum(
        "pjrc,krpc->jk", centred_frames, eigen_blk, precision=lax.Precision.HIGHEST
    )
    fit_rhs = sum_by_exchange(partial_value, "pix", pix_count) / npix
    weights = solve_normal(normal, fit_rhs)
    estimate = mean_blk.transpose(1, 0, 2)[:, None] + jnp.einsum(
        "jk,krpc->pjrc", weights, eigen_blk, precision=lax.Precision.HIGHEST
    )
    tiles_out = tiles / jnp.maximum(estimate, floor_value)
    back = lax.all_to_all(tiles_out, "pix", 0, 0, tiled=True)
    result = back.transpose(1, 0, 2, 3).reshape(angle_count, rows_all, cols_here)
    return result


def solution(mesh):
    in_specs = (P(None, "pix", "ang"), P("ang", None, "pix"), P())
    out_specs = P("ang", None, "pix")
    return jax.shard_map(shards, mesh=mesh, in_specs=in_specs, out_specs=out_specs, check_vma=False)
```

```python
import jax
import jax.numpy as jnp
from jax import lax
from jax.sharding import PartitionSpec as P
from jax.experimental import pallas as pl

SUBSPACE = 2


floor_value = 0.2


def orthonormal(grown):
    correlation = jnp.dot(grown.T, grown, precision=lax.Precision.HIGHEST)
    lower = jnp.linalg.cholesky(correlation)
    return jax.scipy.linalg.solve_triangular(lower, grown.T, lower=True).T


def solve_normal(normal, fit_rhs):
    factor = jnp.linalg.cholesky(normal)
    return jax.scipy.linalg.cho_solve((factor, True), fit_rhs.T).T


def sum_by_exchange(rows, axes, count):
    total, width = rows.shape
    pieces = lax.all_to_all(rows.reshape(count, total // count, width), axes, 0, 0, tiled=True)
    block = jnp.sum(pieces, axis=0)
    spread = jnp.broadcast_to(block[None], (count,) + block.shape)
    gathered = lax.all_to_all(spread, axes, 0, 0, tiled=True)
    return gathered.reshape(total, width)


def _project_kernel(lhs_ref, rhs_ref, out_ref):
    lhs = lhs_ref[...]
    for row in range(rhs_ref.shape[1]):
        out_ref[:, row, :] = jnp.dot(
            lhs, rhs_ref[:, row, :], precision=lax.Precision.HIGHEST,
            preferred_element_type=jnp.float32,
        )


def project_rows(lhs, rhs):
    m, k = lhs.shape
    _, rows, width = rhs.shape
    return pl.pallas_call(
        _project_kernel,
        grid=(1,),
        in_specs=[
            pl.BlockSpec((m, k), lambda r: (0, 0)),
            pl.BlockSpec((k, rows, width), lambda r: (0, 0, 0)),
        ],
        out_specs=pl.BlockSpec((m, rows, width), lambda r: (0, 0, 0)),
        out_shape=jax.ShapeDtypeStruct((m, rows, width), jnp.float32),
    )(lhs, rhs)


def shards(flats, projections, start_basis):
    frames_here, rows_dev, cols_dev = flats.shape
    ang_count = lax.axis_size("ang")
    pix_count = lax.axis_size("pix")
    npix = rows_dev * cols_dev * ang_count * pix_count
    angle_count, rows_all, cols_here = projections.shape

    tiles_in = projections.reshape(angle_count, pix_count, rows_dev, cols_here).transpose(1, 0, 2, 3)
    tiles = lax.all_to_all(tiles_in, "pix", 0, 0, tiled=True)

    mean_flat = jnp.mean(flats, axis=0)
    centered_rows = flats - mean_flat
    centered = centered_rows.reshape(frames_here, -1)
    local_gram = jnp.dot(centered, centered.T, precision=lax.Precision.HIGHEST)
    device_count = ang_count * pix_count
    gram_rows = local_gram.reshape(device_count, -1)
    gram = sum_by_exchange(gram_rows, ("ang", "pix"), device_count).reshape(frames_here, frames_here) / npix
    basis = start_basis
    for turn in range(SUBSPACE):
        basis = orthonormal(jnp.dot(gram, basis, precision=lax.Precision.HIGHEST))
    eigen_3d = project_rows(basis.T, centered_rows)
    eigen_flats = eigen_3d.reshape(basis.shape[1], -1)
    normal = jnp.dot(
        basis.T,
        jnp.dot(gram, basis, precision=lax.Precision.HIGHEST),
        precision=lax.Precision.HIGHEST,
    )
    eigen_count = eigen_flats.shape[0]
    eigen_rows = lax.all_gather(
        eigen_3d, "ang", axis=2, tiled=True
    )
    mean_rows = lax.all_gather(mean_flat, "ang", axis=1, tiled=True)
    eigen_blk = eigen_rows.reshape(eigen_count, rows_dev, pix_count, cols_here)
    mean_blk = mean_rows.reshape(rows_dev, pix_count, cols_here)
    centred_frames = tiles - mean_blk.transpose(1, 0, 2)[:, None]
    partial_value = jnp.einsum(
        "pjrc,krpc->jk", centred_frames, eigen_blk, precision=lax.Precision.HIGH
    )
    fit_rhs = sum_by_exchange(partial_value, "pix", pix_count) / npix
    weights = solve_normal(normal, fit_rhs)
    estimate = mean_blk.transpose(1, 0, 2)[:, None] + jnp.einsum(
        "jk,krpc->pjrc", weights, eigen_blk, precision=lax.Precision.HIGH
    )
    tiles_out = tiles / jnp.maximum(estimate, floor_value)
    back = lax.all_to_all(tiles_out, "pix", 0, 0, tiled=True)
    result = back.transpose(1, 0, 2, 3).reshape(angle_count, rows_all, cols_here)
    return result


def solution(mesh):
    in_specs = (P(None, "pix", "ang"), P("ang", None, "pix"), P())
    out_specs = P("ang", None, "pix")
    return jax.shard_map(shards, mesh=mesh, in_specs=in_specs, out_specs=out_specs, check_vma=False)
```

```python
import jax
import jax.numpy as jnp
from jax import lax
from jax.sharding import PartitionSpec as P
from jax.experimental import pallas as pl

SUBSPACE = 2


floor_value = 0.2


def orthonormal(grown):
    correlation = jnp.dot(grown.T, grown, precision=lax.Precision.HIGHEST)
    lower = jnp.linalg.cholesky(correlation)
    return jax.scipy.linalg.solve_triangular(lower, grown.T, lower=True).T


def solve_normal(normal, fit_rhs):
    factor = jnp.linalg.cholesky(normal)
    return jax.scipy.linalg.cho_solve((factor, True), fit_rhs.T).T


def sum_by_exchange(rows, axes, count):
    total, width = rows.shape
    pieces = lax.all_to_all(rows.reshape(count, total // count, width), axes, 0, 0, tiled=True)
    block = jnp.sum(pieces, axis=0)
    spread = jnp.broadcast_to(block[None], (count,) + block.shape)
    gathered = lax.all_to_all(spread, axes, 0, 0, tiled=True)
    return gathered.reshape(total, width)


def _project_kernel(lhs_ref, rhs_ref, out_ref):
    lhs = lhs_ref[...]
    for row in range(rhs_ref.shape[1]):
        out_ref[:, row, :] = jnp.dot(
            lhs, rhs_ref[:, row, :], precision=lax.Precision.HIGHEST,
            preferred_element_type=jnp.float32,
        )


def project_rows(lhs, rhs):
    m, k = lhs.shape
    _, rows, width = rhs.shape
    return pl.pallas_call(
        _project_kernel,
        grid=(1,),
        in_specs=[
            pl.BlockSpec((m, k), lambda r: (0, 0)),
            pl.BlockSpec((k, rows, width), lambda r: (0, 0, 0)),
        ],
        out_specs=pl.BlockSpec((m, rows, width), lambda r: (0, 0, 0)),
        out_shape=jax.ShapeDtypeStruct((m, rows, width), jnp.float32),
    )(lhs, rhs)


def shards(flats, projections, start_basis):
    frames_here, rows_dev, cols_dev = flats.shape
    ang_count = lax.axis_size("ang")
    pix_count = lax.axis_size("pix")
    npix = rows_dev * cols_dev * ang_count * pix_count
    angle_count, rows_all, cols_here = projections.shape

    tiles_in = projections.reshape(angle_count, pix_count, rows_dev, cols_here).transpose(1, 0, 2, 3)
    tiles = lax.all_to_all(tiles_in, "pix", 0, 0, tiled=True)

    mean_flat = jnp.mean(flats, axis=0)
    centered_rows = flats - mean_flat
    centered = centered_rows.reshape(frames_here, -1)
    local_gram = jnp.dot(centered, centered.T, precision=lax.Precision.HIGHEST)
    tiles, local_gram = lax.optimization_barrier((tiles, local_gram))
    device_count = ang_count * pix_count
    sub_blocks = cols_dev // cols_here
    by_groups = tiles.reshape(ang_count, sub_blocks, angle_count, rows_dev, cols_here)
    by_pixels = lax.all_to_all(by_groups, "ang", 0, 0, tiled=True)
    gram_rows = local_gram.reshape(device_count, -1)
    gram = sum_by_exchange(gram_rows, ("ang", "pix"), device_count).reshape(frames_here, frames_here) / npix
    basis = start_basis
    for turn in range(SUBSPACE):
        basis = orthonormal(jnp.dot(gram, basis, precision=lax.Precision.HIGHEST))
    by_pixels, basis = lax.optimization_barrier((by_pixels, basis))
    mean_local = mean_flat.reshape(rows_dev, sub_blocks, cols_here)
    local_products = jnp.einsum(
        "asjrc,frsc->ajf",
        by_pixels - mean_local.transpose(1, 0, 2)[None, :, None],
        centered_rows.reshape(frames_here, rows_dev, sub_blocks, cols_here),
        precision=lax.Precision.HIGHEST,
    ).reshape(ang_count * angle_count, frames_here)
    products = sum_by_exchange(local_products, ("ang", "pix"), device_count)
    mine = lax.dynamic_slice_in_dim(products, lax.axis_index("ang") * angle_count, angle_count, 0)
    eigen_3d = project_rows(basis.T, centered_rows)
    eigen_flats = eigen_3d.reshape(basis.shape[1], -1)
    normal = jnp.dot(
        basis.T,
        jnp.dot(gram, basis, precision=lax.Precision.HIGHEST),
        precision=lax.Precision.HIGHEST,
    )
    eigen_count = eigen_flats.shape[0]
    eigen_rows = lax.all_gather(
        eigen_3d, "ang", axis=2, tiled=True
    )
    mean_rows = lax.all_gather(mean_flat, "ang", axis=1, tiled=True)
    eigen_blk = eigen_rows.reshape(eigen_count, rows_dev, pix_count, cols_here)
    mean_blk = mean_rows.reshape(rows_dev, pix_count, cols_here)
    fit_rhs = jnp.dot(mine, basis, precision=lax.Precision.HIGHEST) / npix
    weights = solve_normal(normal, fit_rhs)
    estimate = mean_blk.transpose(1, 0, 2)[:, None] + jnp.einsum(
        "jk,krpc->pjrc", weights, eigen_blk, precision=lax.Precision.HIGH
    )
    tiles_out = tiles / jnp.maximum(estimate, floor_value)
    back = lax.all_to_all(tiles_out, "pix", 0, 0, tiled=True)
    result = back.transpose(1, 0, 2, 3).reshape(angle_count, rows_all, cols_here)
    return result


def solution(mesh):
    in_specs = (P(None, "pix", "ang"), P("ang", None, "pix"), P())
    out_specs = P("ang", None, "pix")
    return jax.shard_map(shards, mesh=mesh, in_specs=in_specs, out_specs=out_specs, check_vma=False)
```

```python
import jax
import jax.numpy as jnp
from jax import lax
from jax.sharding import PartitionSpec as P
from jax.experimental import pallas as pl

SUBSPACE = 2


floor_value = 0.2


def orthonormal(grown):
    correlation = jnp.dot(grown.T, grown, precision=lax.Precision.HIGHEST)
    lower = jnp.linalg.cholesky(correlation)
    return jax.scipy.linalg.solve_triangular(lower, grown.T, lower=True).T


def solve_normal(normal, fit_rhs):
    factor = jnp.linalg.cholesky(normal)
    return jax.scipy.linalg.cho_solve((factor, True), fit_rhs.T).T


def sum_by_exchange(rows, axes, count):
    total, width = rows.shape
    pieces = lax.all_to_all(rows.reshape(count, total // count, width), axes, 0, 0, tiled=True)
    block = jnp.sum(pieces, axis=0)
    spread = jnp.broadcast_to(block[None], (count,) + block.shape)
    gathered = lax.all_to_all(spread, axes, 0, 0, tiled=True)
    return gathered.reshape(total, width)


def _project_kernel(lhs_ref, rhs_ref, out_ref):
    lhs = lhs_ref[...]
    for row in range(rhs_ref.shape[1]):
        out_ref[:, row, :] = jnp.dot(
            lhs, rhs_ref[:, row, :], precision=lax.Precision.HIGH,
            preferred_element_type=jnp.float32,
        )


def project_rows(lhs, rhs):
    m, k = lhs.shape
    _, rows, width = rhs.shape
    return pl.pallas_call(
        _project_kernel,
        grid=(1,),
        in_specs=[
            pl.BlockSpec((m, k), lambda r: (0, 0)),
            pl.BlockSpec((k, rows, width), lambda r: (0, 0, 0)),
        ],
        out_specs=pl.BlockSpec((m, rows, width), lambda r: (0, 0, 0)),
        out_shape=jax.ShapeDtypeStruct((m, rows, width), jnp.float32),
    )(lhs, rhs)


def shards(flats, projections, start_basis):
    frames_here, rows_dev, cols_dev = flats.shape
    ang_count = lax.axis_size("ang")
    pix_count = lax.axis_size("pix")
    npix = rows_dev * cols_dev * ang_count * pix_count
    angle_count, rows_all, cols_here = projections.shape

    tiles_in = projections.reshape(angle_count, pix_count, rows_dev, cols_here).transpose(1, 0, 2, 3)
    tiles = lax.all_to_all(tiles_in, "pix", 0, 0, tiled=True)

    mean_flat = jnp.mean(flats, axis=0)
    centered_rows = flats - mean_flat
    centered = centered_rows.reshape(frames_here, -1)
    local_gram = jnp.dot(centered, centered.T, precision=lax.Precision.HIGHEST)
    device_count = ang_count * pix_count
    gram_rows = local_gram.reshape(device_count, -1)
    gram = sum_by_exchange(gram_rows, ("ang", "pix"), device_count).reshape(frames_here, frames_here) / npix
    basis = start_basis
    for turn in range(SUBSPACE):
        basis = orthonormal(jnp.dot(gram, basis, precision=lax.Precision.HIGHEST))
    eigen_3d = project_rows(basis.T, centered_rows)
    eigen_flats = eigen_3d.reshape(basis.shape[1], -1)
    normal = jnp.dot(
        basis.T,
        jnp.dot(gram, basis, precision=lax.Precision.HIGHEST),
        precision=lax.Precision.HIGHEST,
    )
    eigen_count = eigen_flats.shape[0]
    eigen_rows = lax.all_gather(
        eigen_3d, "ang", axis=2, tiled=True
    )
    mean_rows = lax.all_gather(mean_flat, "ang", axis=1, tiled=True)
    eigen_blk = eigen_rows.reshape(eigen_count, rows_dev, pix_count, cols_here)
    mean_blk = mean_rows.reshape(rows_dev, pix_count, cols_here)
    centred_frames = tiles - mean_blk.transpose(1, 0, 2)[:, None]
    partial_value = jnp.einsum(
        "pjrc,krpc->jk", centred_frames, eigen_blk, precision=lax.Precision.HIGH
    )
    fit_rhs = sum_by_exchange(partial_value, "pix", pix_count) / npix
    weights = solve_normal(normal, fit_rhs)
    estimate = mean_blk.transpose(1, 0, 2)[:, None] + jnp.einsum(
        "jk,krpc->pjrc", weights, eigen_blk, precision=lax.Precision.HIGH
    )
    tiles_out = tiles / jnp.maximum(estimate, floor_value)
    back = lax.all_to_all(tiles_out, "pix", 0, 0, tiled=True)
    result = back.transpose(1, 0, 2, 3).reshape(angle_count, rows_all, cols_here)
    return result


def solution(mesh):
    in_specs = (P(None, "pix", "ang"), P("ang", None, "pix"), P())
    out_specs = P("ang", None, "pix")
    return jax.shard_map(shards, mesh=mesh, in_specs=in_specs, out_specs=out_specs, check_vma=False)
```

```python
import jax
import jax.numpy as jnp
from jax import lax
from jax.sharding import PartitionSpec as P
from jax.experimental import pallas as pl

SUBSPACE = 2


floor_value = 0.2


def orthonormal(grown):
    correlation = jnp.dot(grown.T, grown, precision=lax.Precision.HIGHEST)
    lower = jnp.linalg.cholesky(correlation)
    return jax.scipy.linalg.solve_triangular(lower, grown.T, lower=True).T


def solve_normal(normal, fit_rhs):
    factor = jnp.linalg.cholesky(normal)
    return jax.scipy.linalg.cho_solve((factor, True), fit_rhs.T).T


def sum_by_exchange(rows, axes, count):
    total, width = rows.shape
    pieces = lax.all_to_all(rows.reshape(count, total // count, width), axes, 0, 0, tiled=True)
    block = jnp.sum(pieces, axis=0)
    spread = jnp.broadcast_to(block[None], (count,) + block.shape)
    gathered = lax.all_to_all(spread, axes, 0, 0, tiled=True)
    return gathered.reshape(total, width)


def _gram_kernel(flats_ref, gram_ref, mean_ref):
    step = pl.program_id(0)

    @pl.when(step == 0)
    def _():
        gram_ref[...] = jnp.zeros_like(gram_ref)

    block = flats_ref[...]
    mean = jnp.sum(block, axis=0) / block.shape[0]
    mean_ref[...] = mean
    total = gram_ref[...]
    for row in range(block.shape[1]):
        centred = block[:, row, :] - mean[row][None, :]
        total += lax.dot_general(
            centred, centred, (((1,), (1,)), ((), ())),
            precision=lax.Precision.HIGHEST, preferred_element_type=jnp.float32,
        )
    gram_ref[...] = total


def frame_gram(flats, width=256):
    frames, rows, cols = flats.shape
    return pl.pallas_call(
        _gram_kernel,
        grid=(cols // width,),
        in_specs=[pl.BlockSpec((frames, rows, width), lambda i: (0, 0, i))],
        out_specs=[
            pl.BlockSpec((frames, frames), lambda i: (0, 0)),
            pl.BlockSpec((rows, width), lambda i: (0, i)),
        ],
        out_shape=[
            jax.ShapeDtypeStruct((frames, frames), jnp.float32),
            jax.ShapeDtypeStruct((rows, cols), jnp.float32),
        ],
    )(flats)


def _project_kernel(lhs_ref, flats_ref, mean_ref, out_ref):
    lhs = lhs_ref[...]
    for row in range(flats_ref.shape[1]):
        centred = flats_ref[:, row, :] - mean_ref[row, :][None, :]
        out_ref[:, row, :] = jnp.dot(
            lhs, centred, precision=lax.Precision.HIGH,
            preferred_element_type=jnp.float32,
        )


def project_rows(lhs, flats, mean):
    m, k = lhs.shape
    _, rows, width = flats.shape
    return pl.pallas_call(
        _project_kernel,
        grid=(1,),
        in_specs=[
            pl.BlockSpec((m, k), lambda r: (0, 0)),
            pl.BlockSpec((k, rows, width), lambda r: (0, 0, 0)),
            pl.BlockSpec((rows, width), lambda r: (0, 0)),
        ],
        out_specs=pl.BlockSpec((m, rows, width), lambda r: (0, 0, 0)),
        out_shape=jax.ShapeDtypeStruct((m, rows, width), jnp.float32),
    )(lhs, flats, mean)


def shards(flats, projections, start_basis):
    frames_here, rows_dev, cols_dev = flats.shape
    ang_count = lax.axis_size("ang")
    pix_count = lax.axis_size("pix")
    npix = rows_dev * cols_dev * ang_count * pix_count
    angle_count, rows_all, cols_here = projections.shape

    tiles_in = projections.reshape(angle_count, pix_count, rows_dev, cols_here).transpose(1, 0, 2, 3)
    tiles = lax.all_to_all(tiles_in, "pix", 0, 0, tiled=True)

    local_gram, mean_flat = frame_gram(flats)
    device_count = ang_count * pix_count
    gram_rows = local_gram.reshape(device_count, -1)
    gram = sum_by_exchange(gram_rows, ("ang", "pix"), device_count).reshape(frames_here, frames_here) / npix
    basis = start_basis
    for turn in range(SUBSPACE):
        basis = orthonormal(jnp.dot(gram, basis, precision=lax.Precision.HIGHEST))
    eigen_3d = project_rows(basis.T, flats, mean_flat)
    eigen_flats = eigen_3d.reshape(basis.shape[1], -1)
    normal = jnp.dot(
        basis.T,
        jnp.dot(gram, basis, precision=lax.Precision.HIGHEST),
        precision=lax.Precision.HIGHEST,
    )
    eigen_count = eigen_flats.shape[0]
    eigen_rows = lax.all_gather(
        eigen_3d, "ang", axis=2, tiled=True
    )
    mean_rows = lax.all_gather(mean_flat, "ang", axis=1, tiled=True)
    eigen_blk = eigen_rows.reshape(eigen_count, rows_dev, pix_count, cols_here)
    mean_blk = mean_rows.reshape(rows_dev, pix_count, cols_here)
    centred_frames = tiles - mean_blk.transpose(1, 0, 2)[:, None]
    partial_value = jnp.einsum(
        "pjrc,krpc->jk", centred_frames, eigen_blk, precision=lax.Precision.HIGH
    )
    fit_rhs = sum_by_exchange(partial_value, "pix", pix_count) / npix
    weights = solve_normal(normal, fit_rhs)
    estimate = mean_blk.transpose(1, 0, 2)[:, None] + jnp.einsum(
        "jk,krpc->pjrc", weights, eigen_blk, precision=lax.Precision.HIGH
    )
    tiles_out = tiles / jnp.maximum(estimate, floor_value)
    back = lax.all_to_all(tiles_out, "pix", 0, 0, tiled=True)
    result = back.transpose(1, 0, 2, 3).reshape(angle_count, rows_all, cols_here)
    return result


def solution(mesh):
    in_specs = (P(None, "pix", "ang"), P("ang", None, "pix"), P())
    out_specs = P("ang", None, "pix")
    return jax.shard_map(shards, mesh=mesh, in_specs=in_specs, out_specs=out_specs, check_vma=False)
```

```python
import jax
import jax.numpy as jnp
from jax import lax
from jax.sharding import PartitionSpec as P
from jax.experimental import pallas as pl

SUBSPACE = 2


floor_value = 0.2


def orthonormal(grown):
    correlation = jnp.dot(grown.T, grown, precision=lax.Precision.HIGHEST)
    lower = jnp.linalg.cholesky(correlation)
    return jax.scipy.linalg.solve_triangular(lower, grown.T, lower=True).T


def solve_normal(normal, fit_rhs):
    factor = jnp.linalg.cholesky(normal)
    return jax.scipy.linalg.cho_solve((factor, True), fit_rhs.T).T


def sum_by_exchange(rows, axes, count):
    total, width = rows.shape
    pieces = lax.all_to_all(rows.reshape(count, total // count, width), axes, 0, 0, tiled=True)
    block = jnp.sum(pieces, axis=0)
    spread = jnp.broadcast_to(block[None], (count,) + block.shape)
    gathered = lax.all_to_all(spread, axes, 0, 0, tiled=True)
    return gathered.reshape(total, width)


def _gram_kernel(flats_ref, gram_ref, mean_ref):
    step = pl.program_id(0)

    @pl.when(step == 0)
    def _():
        gram_ref[...] = jnp.zeros_like(gram_ref)

    block = flats_ref[...]
    mean = jnp.sum(block, axis=0) / block.shape[0]
    mean_ref[...] = mean
    total = gram_ref[...]
    for row in range(block.shape[1]):
        centred = block[:, row, :] - mean[row][None, :]
        total += lax.dot_general(
            centred, centred, (((1,), (1,)), ((), ())),
            precision=lax.Precision.HIGHEST, preferred_element_type=jnp.float32,
        )
    gram_ref[...] = total


def frame_gram(flats, width=256):
    frames, rows, cols = flats.shape
    return pl.pallas_call(
        _gram_kernel,
        grid=(cols // width,),
        in_specs=[pl.BlockSpec((frames, rows, width), lambda i: (0, 0, i))],
        out_specs=[
            pl.BlockSpec((frames, frames), lambda i: (0, 0)),
            pl.BlockSpec((rows, width), lambda i: (0, i)),
        ],
        out_shape=[
            jax.ShapeDtypeStruct((frames, frames), jnp.float32),
            jax.ShapeDtypeStruct((rows, cols), jnp.float32),
        ],
    )(flats)


def _project_kernel(lhs_ref, flats_ref, mean_ref, out_ref):
    lhs = lhs_ref[...]
    for row in range(flats_ref.shape[1]):
        centred = flats_ref[:, row, :] - mean_ref[row, :][None, :]
        out_ref[:, row, :] = jnp.dot(
            lhs, centred, precision=lax.Precision.HIGH,
            preferred_element_type=jnp.float32,
        )


def project_rows(lhs, flats, mean):
    m, k = lhs.shape
    _, rows, width = flats.shape
    return pl.pallas_call(
        _project_kernel,
        grid=(1,),
        in_specs=[
            pl.BlockSpec((m, k), lambda r: (0, 0)),
            pl.BlockSpec((k, rows, width), lambda r: (0, 0, 0)),
            pl.BlockSpec((rows, width), lambda r: (0, 0)),
        ],
        out_specs=pl.BlockSpec((m, rows, width), lambda r: (0, 0, 0)),
        out_shape=jax.ShapeDtypeStruct((m, rows, width), jnp.float32),
    )(lhs, flats, mean)


def shards(flats, projections, start_basis):
    frames_here, rows_dev, cols_dev = flats.shape
    ang_count = lax.axis_size("ang")
    pix_count = lax.axis_size("pix")
    npix = rows_dev * cols_dev * ang_count * pix_count
    angle_count, rows_all, cols_here = projections.shape

    tiles_in = projections.reshape(angle_count, pix_count, rows_dev, cols_here).transpose(1, 0, 2, 3)
    tiles = lax.all_to_all(tiles_in, "pix", 0, 0, tiled=True)

    local_gram, mean_flat = frame_gram(flats)
    device_count = ang_count * pix_count
    gram_rows = local_gram.reshape(device_count, -1)
    gram = sum_by_exchange(gram_rows, ("ang", "pix"), device_count).reshape(frames_here, frames_here) / npix
    basis = start_basis
    for turn in range(SUBSPACE):
        basis = orthonormal(jnp.dot(gram, basis, precision=lax.Precision.HIGHEST))
    eigen_3d = project_rows(basis.T, flats, mean_flat)
    eigen_flats = eigen_3d.reshape(basis.shape[1], -1)
    normal = jnp.dot(
        basis.T,
        jnp.dot(gram, basis, precision=lax.Precision.HIGHEST),
        precision=lax.Precision.HIGHEST,
    )
    eigen_count = eigen_flats.shape[0]
    own = jnp.concatenate([eigen_3d, mean_flat[None]], axis=0)
    here = lax.axis_index("ang")
    pieces = [(here, own)]
    for shift in range(1, ang_count):
        moved = lax.ppermute(own, "ang", [(i, (i + shift) % ang_count) for i in range(ang_count)])
        pieces.append(((here - shift) % ang_count, moved))
    group_blocks = cols_dev // cols_here
    parts = []
    for group, piece in pieces:
        piece = piece.reshape(eigen_count + 1, rows_dev, group_blocks, cols_here)
        frames_g = lax.dynamic_slice_in_dim(tiles, group * group_blocks, group_blocks, 0)
        mean_g = piece[eigen_count].transpose(1, 0, 2)[:, None]
        parts.append((group, piece[:eigen_count], mean_g, frames_g))
    partial_value = sum(
        jnp.einsum("pjrc,krpc->jk", frames_g - mean_g, eigen_g, precision=lax.Precision.HIGH)
        for group, eigen_g, mean_g, frames_g in parts
    )
    fit_rhs = sum_by_exchange(partial_value, "pix", pix_count) / npix
    weights = solve_normal(normal, fit_rhs)
    tiles_out = jnp.zeros_like(tiles)
    for group, eigen_g, mean_g, frames_g in parts:
        estimate = mean_g + jnp.einsum(
            "jk,krpc->pjrc", weights, eigen_g, precision=lax.Precision.HIGH
        )
        tiles_out = lax.dynamic_update_slice_in_dim(
            tiles_out, frames_g / jnp.maximum(estimate, floor_value), group * group_blocks, 0
        )
    back = lax.all_to_all(tiles_out, "pix", 0, 0, tiled=True)
    result = back.transpose(1, 0, 2, 3).reshape(angle_count, rows_all, cols_here)
    return result


def solution(mesh):
    in_specs = (P(None, "pix", "ang"), P("ang", None, "pix"), P())
    out_specs = P("ang", None, "pix")
    return jax.shard_map(shards, mesh=mesh, in_specs=in_specs, out_specs=out_specs, check_vma=False)
```

```python
import jax
import jax.numpy as jnp
from jax import lax
from jax.sharding import PartitionSpec as P
from jax.experimental import pallas as pl

SUBSPACE = 2


floor_value = 0.2


def orthonormal(grown):
    correlation = jnp.dot(grown.T, grown, precision=lax.Precision.HIGHEST)
    lower = jnp.linalg.cholesky(correlation)
    return jax.scipy.linalg.solve_triangular(lower, grown.T, lower=True).T


def solve_normal(normal, fit_rhs):
    factor = jnp.linalg.cholesky(normal)
    return jax.scipy.linalg.cho_solve((factor, True), fit_rhs.T).T


def sum_by_exchange(rows, axes, count):
    total, width = rows.shape
    pieces = lax.all_to_all(rows.reshape(count, total // count, width), axes, 0, 0, tiled=True)
    block = jnp.sum(pieces, axis=0)
    spread = jnp.broadcast_to(block[None], (count,) + block.shape)
    gathered = lax.all_to_all(spread, axes, 0, 0, tiled=True)
    return gathered.reshape(total, width)


def _gram_kernel(flats_ref, gram_ref, mean_ref):
    step = pl.program_id(0)

    @pl.when(step == 0)
    def _():
        gram_ref[...] = jnp.zeros_like(gram_ref)

    block = flats_ref[...]
    mean = jnp.sum(block, axis=0) / block.shape[0]
    mean_ref[...] = mean
    total = gram_ref[...]
    for row in range(block.shape[1]):
        centred = block[:, row, :] - mean[row][None, :]
        total += lax.dot_general(
            centred, centred, (((1,), (1,)), ((), ())),
            precision=lax.Precision.HIGHEST, preferred_element_type=jnp.float32,
        )
    gram_ref[...] = total


def frame_gram(flats, width=256):
    frames, rows, cols = flats.shape
    return pl.pallas_call(
        _gram_kernel,
        grid=(cols // width,),
        in_specs=[pl.BlockSpec((frames, rows, width), lambda i: (0, 0, i))],
        out_specs=[
            pl.BlockSpec((frames, frames), lambda i: (0, 0)),
            pl.BlockSpec((rows, width), lambda i: (0, i)),
        ],
        out_shape=[
            jax.ShapeDtypeStruct((frames, frames), jnp.float32),
            jax.ShapeDtypeStruct((rows, cols), jnp.float32),
        ],
    )(flats)


def _project_kernel(lhs_ref, flats_ref, mean_ref, out_ref):
    lhs = lhs_ref[...]
    for row in range(flats_ref.shape[1]):
        centred = flats_ref[:, row, :] - mean_ref[row, :][None, :]
        out_ref[:, row, :] = jnp.dot(
            lhs, centred, precision=lax.Precision.HIGH,
            preferred_element_type=jnp.float32,
        )


def project_rows(lhs, flats, mean):
    m, k = lhs.shape
    _, rows, width = flats.shape
    return pl.pallas_call(
        _project_kernel,
        grid=(1,),
        in_specs=[
            pl.BlockSpec((m, k), lambda r: (0, 0)),
            pl.BlockSpec((k, rows, width), lambda r: (0, 0, 0)),
            pl.BlockSpec((rows, width), lambda r: (0, 0)),
        ],
        out_specs=pl.BlockSpec((m, rows, width), lambda r: (0, 0, 0)),
        out_shape=jax.ShapeDtypeStruct((m, rows, width), jnp.float32),
    )(lhs, flats, mean)


def shards(flats, projections, start_basis):
    frames_here, rows_dev, cols_dev = flats.shape
    ang_count = lax.axis_size("ang")
    pix_count = lax.axis_size("pix")
    npix = rows_dev * cols_dev * ang_count * pix_count
    angle_count, rows_all, cols_here = projections.shape

    tiles_in = projections.reshape(angle_count, pix_count, rows_dev, cols_here).transpose(1, 0, 2, 3)
    tiles = lax.all_to_all(tiles_in, "pix", 0, 0, tiled=True)

    local_gram, mean_flat = frame_gram(flats)
    device_count = ang_count * pix_count
    gram_rows = local_gram.reshape(device_count, -1)
    gram = sum_by_exchange(gram_rows, ("ang", "pix"), device_count).reshape(frames_here, frames_here) / npix
    basis = start_basis
    for turn in range(SUBSPACE):
        basis = orthonormal(jnp.dot(gram, basis, precision=lax.Precision.HIGHEST))
    eigen_3d = project_rows(basis.T, flats, mean_flat)
    eigen_flats = eigen_3d.reshape(basis.shape[1], -1)
    normal = jnp.dot(
        basis.T,
        jnp.dot(gram, basis, precision=lax.Precision.HIGHEST),
        precision=lax.Precision.HIGHEST,
    )
    eigen_count = eigen_flats.shape[0]
    here = lax.axis_index("ang")
    group_blocks = cols_dev // cols_here
    half = eigen_count // 2

    def shift(value, step):
        return lax.ppermute(value, "ang", [(i, (i + step) % ang_count) for i in range(ang_count)])

    eigen_up, eigen_down = shift(eigen_3d, 1), shift(eigen_3d, -1)
    mean_up, mean_down = shift(mean_flat, 1), shift(mean_flat, -1)
    far_low, far_high = shift(eigen_up[:half], 1), shift(eigen_down[half:], -1)
    mean_far = shift(mean_up, 1)
    sources = [
        (here, [(0, eigen_3d)], mean_flat),
        ((here - 1) % ang_count, [(0, eigen_up)], mean_up),
        ((here + 1) % ang_count, [(0, eigen_down)], mean_down),
        ((here + 2) % ang_count, [(0, far_low), (half, far_high)], mean_far),
    ]
    parts = []
    for group, eigen_parts, mean_piece in sources:
        frames_g = lax.dynamic_slice_in_dim(tiles, group * group_blocks, group_blocks, 0)
        mean_g = mean_piece.reshape(rows_dev, group_blocks, cols_here).transpose(1, 0, 2)[:, None]
        views = [
            (start, piece.reshape(piece.shape[0], rows_dev, group_blocks, cols_here))
            for start, piece in eigen_parts
        ]
        parts.append((group, views, mean_g, frames_g))
    partial_value = 0.0
    for group, views, mean_g, frames_g in parts:
        centred_g = frames_g - mean_g
        pieces = [
            jnp.einsum("pjrc,krpc->jk", centred_g, view, precision=lax.Precision.HIGH)
            for start, view in views
        ]
        partial_value = partial_value + jnp.concatenate(pieces, axis=1)
    fit_rhs = sum_by_exchange(partial_value, "pix", pix_count) / npix
    weights = solve_normal(normal, fit_rhs)
    tiles_out = jnp.zeros_like(tiles)
    for group, views, mean_g, frames_g in parts:
        estimate = mean_g
        for start, view in views:
            estimate = estimate + jnp.einsum(
                "jk,krpc->pjrc", weights[:, start:start + view.shape[0]], view,
                precision=lax.Precision.HIGH,
            )
        tiles_out = lax.dynamic_update_slice_in_dim(
            tiles_out, frames_g / jnp.maximum(estimate, floor_value), group * group_blocks, 0
        )
    back = lax.all_to_all(tiles_out, "pix", 0, 0, tiled=True)
    result = back.transpose(1, 0, 2, 3).reshape(angle_count, rows_all, cols_here)
    return result


def solution(mesh):
    in_specs = (P(None, "pix", "ang"), P("ang", None, "pix"), P())
    out_specs = P("ang", None, "pix")
    return jax.shard_map(shards, mesh=mesh, in_specs=in_specs, out_specs=out_specs, check_vma=False)
```

```python
import jax
import jax.numpy as jnp
from jax import lax
from jax.sharding import PartitionSpec as P
from jax.experimental import pallas as pl

SUBSPACE = 2


floor_value = 0.2


def orthonormal(grown):
    correlation = jnp.dot(grown.T, grown, precision=lax.Precision.HIGHEST)
    lower = jnp.linalg.cholesky(correlation)
    return jax.scipy.linalg.solve_triangular(lower, grown.T, lower=True).T


def solve_normal(normal, fit_rhs):
    factor = jnp.linalg.cholesky(normal)
    return jax.scipy.linalg.cho_solve((factor, True), fit_rhs.T).T


def sum_by_exchange(rows, axes, count):
    total, width = rows.shape
    pieces = lax.all_to_all(rows.reshape(count, total // count, width), axes, 0, 0, tiled=True)
    block = jnp.sum(pieces, axis=0)
    spread = jnp.broadcast_to(block[None], (count,) + block.shape)
    gathered = lax.all_to_all(spread, axes, 0, 0, tiled=True)
    return gathered.reshape(total, width)


def _gram_kernel(flats_ref, gram_ref, mean_ref):
    step = pl.program_id(0)

    @pl.when(step == 0)
    def _():
        gram_ref[...] = jnp.zeros_like(gram_ref)

    block = flats_ref[...]
    mean = jnp.sum(block, axis=0) / block.shape[0]
    mean_ref[...] = mean
    total = gram_ref[...]
    for row in range(block.shape[1]):
        centred = block[:, row, :] - mean[row][None, :]
        total += lax.dot_general(
            centred, centred, (((1,), (1,)), ((), ())),
            precision=lax.Precision.HIGHEST, preferred_element_type=jnp.float32,
        )
    gram_ref[...] = total


def frame_gram(flats, width=256):
    frames, rows, cols = flats.shape
    return pl.pallas_call(
        _gram_kernel,
        grid=(cols // width,),
        in_specs=[pl.BlockSpec((frames, rows, width), lambda i: (0, 0, i))],
        out_specs=[
            pl.BlockSpec((frames, frames), lambda i: (0, 0)),
            pl.BlockSpec((rows, width), lambda i: (0, i)),
        ],
        out_shape=[
            jax.ShapeDtypeStruct((frames, frames), jnp.float32),
            jax.ShapeDtypeStruct((rows, cols), jnp.float32),
        ],
    )(flats)


def _project_kernel(lhs_ref, flats_ref, mean_ref, out_ref):
    lhs = lhs_ref[...]
    for row in range(flats_ref.shape[1]):
        centred = flats_ref[:, row, :] - mean_ref[row, :][None, :]
        out_ref[:, row, :] = jnp.dot(
            lhs, centred, precision=lax.Precision.HIGH,
            preferred_element_type=jnp.float32,
        )


def project_rows(lhs, flats, mean):
    m, k = lhs.shape
    _, rows, width = flats.shape
    return pl.pallas_call(
        _project_kernel,
        grid=(1,),
        in_specs=[
            pl.BlockSpec((m, k), lambda r: (0, 0)),
            pl.BlockSpec((k, rows, width), lambda r: (0, 0, 0)),
            pl.BlockSpec((rows, width), lambda r: (0, 0)),
        ],
        out_specs=pl.BlockSpec((m, rows, width), lambda r: (0, 0, 0)),
        out_shape=jax.ShapeDtypeStruct((m, rows, width), jnp.float32),
    )(lhs, flats, mean)


def shards(flats, projections, start_basis):
    frames_here, rows_dev, cols_dev = flats.shape
    ang_count = lax.axis_size("ang")
    pix_count = lax.axis_size("pix")
    npix = rows_dev * cols_dev * ang_count * pix_count
    angle_count, rows_all, cols_here = projections.shape

    tiles_in = projections.reshape(angle_count, pix_count, rows_dev, cols_here).transpose(1, 0, 2, 3)
    tiles = lax.all_to_all(tiles_in, "pix", 0, 0, tiled=True)

    local_gram, mean_flat = frame_gram(flats)
    device_count = ang_count * pix_count
    gram_rows = local_gram.reshape(device_count, -1)
    gram = sum_by_exchange(gram_rows, ("ang", "pix"), device_count).reshape(frames_here, frames_here) / npix
    basis = start_basis
    for turn in range(SUBSPACE):
        basis = orthonormal(jnp.dot(gram, basis, precision=lax.Precision.HIGHEST))
    eigen_3d = project_rows(basis.T, flats, mean_flat)
    eigen_flats = eigen_3d.reshape(basis.shape[1], -1)
    normal = jnp.dot(
        basis.T,
        jnp.dot(gram, basis, precision=lax.Precision.HIGHEST),
        precision=lax.Precision.HIGHEST,
    )
    eigen_count = eigen_flats.shape[0]
    eigen_rows = lax.all_gather(
        eigen_3d, "ang", axis=2, tiled=True
    )
    mean_rows = lax.all_gather(mean_flat, "ang", axis=1, tiled=True)
    group_blocks = cols_dev // cols_here
    eigen_groups = eigen_rows.reshape(eigen_count, rows_dev, ang_count, group_blocks, cols_here)
    mean_groups = mean_rows.reshape(rows_dev, ang_count, group_blocks, cols_here)
    parts = []
    for group in range(ang_count):
        frames_g = tiles[group * group_blocks:(group + 1) * group_blocks]
        mean_g = mean_groups[:, group].transpose(1, 0, 2)[:, None]
        parts.append((eigen_groups[:, :, group], mean_g, frames_g))
    partial_value = sum(
        jnp.einsum("pjrc,krpc->jk", frames_g - mean_g, eigen_g, precision=lax.Precision.HIGH)
        for eigen_g, mean_g, frames_g in parts
    )
    fit_rhs = sum_by_exchange(partial_value, "pix", pix_count) / npix
    weights = solve_normal(normal, fit_rhs)
    outs = []
    for eigen_g, mean_g, frames_g in parts:
        estimate = mean_g + jnp.einsum(
            "jk,krpc->pjrc", weights, eigen_g, precision=lax.Precision.HIGH
        )
        outs.append(frames_g / jnp.maximum(estimate, floor_value))
    tiles_out = jnp.concatenate(outs, axis=0)
    back = lax.all_to_all(tiles_out, "pix", 0, 0, tiled=True)
    result = back.transpose(1, 0, 2, 3).reshape(angle_count, rows_all, cols_here)
    return result


def solution(mesh):
    in_specs = (P(None, "pix", "ang"), P("ang", None, "pix"), P())
    out_specs = P("ang", None, "pix")
    return jax.shard_map(shards, mesh=mesh, in_specs=in_specs, out_specs=out_specs, check_vma=False)
```

```python
import jax
import jax.numpy as jnp
from jax import lax
from jax.sharding import PartitionSpec as P
from jax.experimental import pallas as pl

SUBSPACE = 2


floor_value = 0.2


def orthonormal(grown):
    correlation = jnp.dot(grown.T, grown, precision=lax.Precision.HIGHEST)
    lower = jnp.linalg.cholesky(correlation)
    return jax.scipy.linalg.solve_triangular(lower, grown.T, lower=True).T


def solve_normal(normal, fit_rhs):
    factor = jnp.linalg.cholesky(normal)
    return jax.scipy.linalg.cho_solve((factor, True), fit_rhs.T).T


def sum_by_exchange(rows, axes, count):
    total, width = rows.shape
    pieces = lax.all_to_all(rows.reshape(count, total // count, width), axes, 0, 0, tiled=True)
    block = jnp.sum(pieces, axis=0)
    spread = jnp.broadcast_to(block[None], (count,) + block.shape)
    gathered = lax.all_to_all(spread, axes, 0, 0, tiled=True)
    return gathered.reshape(total, width)


def _gram_kernel(flats_ref, gram_ref, mean_ref):
    step = pl.program_id(0)

    @pl.when(step == 0)
    def _():
        gram_ref[...] = jnp.zeros_like(gram_ref)

    block = flats_ref[...]
    mean = jnp.sum(block, axis=0) / block.shape[0]
    mean_ref[...] = mean
    total = gram_ref[...]
    for row in range(block.shape[1]):
        centred = block[:, row, :] - mean[row][None, :]
        total += lax.dot_general(
            centred, centred, (((1,), (1,)), ((), ())),
            precision=lax.Precision.HIGHEST, preferred_element_type=jnp.float32,
        )
    gram_ref[...] = total


def frame_gram(flats, width=256):
    frames, rows, cols = flats.shape
    return pl.pallas_call(
        _gram_kernel,
        grid=(cols // width,),
        in_specs=[pl.BlockSpec((frames, rows, width), lambda i: (0, 0, i))],
        out_specs=[
            pl.BlockSpec((frames, frames), lambda i: (0, 0)),
            pl.BlockSpec((rows, width), lambda i: (0, i)),
        ],
        out_shape=[
            jax.ShapeDtypeStruct((frames, frames), jnp.float32),
            jax.ShapeDtypeStruct((rows, cols), jnp.float32),
        ],
    )(flats)


def _project_kernel(lhs_ref, flats_ref, mean_ref, out_ref):
    lhs = lhs_ref[...]
    for row in range(flats_ref.shape[1]):
        centred = flats_ref[:, row, :] - mean_ref[row, :][None, :]
        out_ref[row] = jnp.dot(
            lhs, centred, precision=lax.Precision.HIGH,
            preferred_element_type=jnp.float32,
        )


def project_rows(lhs, flats, mean):
    m, k = lhs.shape
    _, rows, width = flats.shape
    return pl.pallas_call(
        _project_kernel,
        grid=(1,),
        in_specs=[
            pl.BlockSpec((m, k), lambda r: (0, 0)),
            pl.BlockSpec((k, rows, width), lambda r: (0, 0, 0)),
            pl.BlockSpec((rows, width), lambda r: (0, 0)),
        ],
        out_specs=pl.BlockSpec((rows, m, width), lambda r: (0, 0, 0)),
        out_shape=jax.ShapeDtypeStruct((rows, m, width), jnp.float32),
    )(lhs, flats, mean)


def shards(flats, projections, start_basis):
    frames_here, rows_dev, cols_dev = flats.shape
    ang_count = lax.axis_size("ang")
    pix_count = lax.axis_size("pix")
    npix = rows_dev * cols_dev * ang_count * pix_count
    angle_count, rows_all, cols_here = projections.shape

    tiles_in = projections.reshape(angle_count, pix_count, rows_dev, cols_here).transpose(1, 0, 2, 3)
    tiles = lax.all_to_all(tiles_in, "pix", 0, 0, tiled=True)

    local_gram, mean_flat = frame_gram(flats)
    device_count = ang_count * pix_count
    gram_rows = local_gram.reshape(device_count, -1)
    gram = sum_by_exchange(gram_rows, ("ang", "pix"), device_count).reshape(frames_here, frames_here) / npix
    basis = start_basis
    for turn in range(SUBSPACE):
        basis = orthonormal(jnp.dot(gram, basis, precision=lax.Precision.HIGHEST))
    eigen_3d = project_rows(basis.T, flats, mean_flat)
    normal = jnp.dot(
        basis.T,
        jnp.dot(gram, basis, precision=lax.Precision.HIGHEST),
        precision=lax.Precision.HIGHEST,
    )
    eigen_count = basis.shape[1]
    eigen_rows = lax.all_gather(
        eigen_3d, "ang", axis=2, tiled=True
    )
    mean_rows = lax.all_gather(mean_flat, "ang", axis=1, tiled=True)
    eigen_blk = eigen_rows.reshape(rows_dev, eigen_count, pix_count, cols_here)
    mean_blk = mean_rows.reshape(rows_dev, pix_count, cols_here)
    centred_frames = tiles - mean_blk.transpose(1, 0, 2)[:, None]
    partial_value = jnp.einsum(
        "pjrc,rkpc->jk", centred_frames, eigen_blk, precision=lax.Precision.HIGH
    )
    fit_rhs = sum_by_exchange(partial_value, "pix", pix_count) / npix
    weights = solve_normal(normal, fit_rhs)
    estimate = mean_blk.transpose(1, 0, 2)[:, None] + jnp.einsum(
        "jk,rkpc->pjrc", weights, eigen_blk, precision=lax.Precision.HIGH
    )
    tiles_out = tiles / jnp.maximum(estimate, floor_value)
    back = lax.all_to_all(tiles_out, "pix", 0, 0, tiled=True)
    result = back.transpose(1, 0, 2, 3).reshape(angle_count, rows_all, cols_here)
    return result


def solution(mesh):
    in_specs = (P(None, "pix", "ang"), P("ang", None, "pix"), P())
    out_specs = P("ang", None, "pix")
    return jax.shard_map(shards, mesh=mesh, in_specs=in_specs, out_specs=out_specs, check_vma=False)
```

```python
import jax
import jax.numpy as jnp
from jax import lax
from jax.sharding import PartitionSpec as P
from jax.experimental import pallas as pl

SUBSPACE = 2


floor_value = 0.2


def orthonormal(grown):
    correlation = jnp.dot(grown.T, grown, precision=lax.Precision.HIGHEST)
    lower = jnp.linalg.cholesky(correlation)
    return jax.scipy.linalg.solve_triangular(lower, grown.T, lower=True).T


def solve_normal(normal, fit_rhs):
    factor = jnp.linalg.cholesky(normal)
    return jax.scipy.linalg.cho_solve((factor, True), fit_rhs.T).T


def sum_by_exchange(rows, axes, count):
    total, width = rows.shape
    pieces = lax.all_to_all(rows.reshape(count, total // count, width), axes, 0, 0, tiled=True)
    block = jnp.sum(pieces, axis=0)
    spread = jnp.broadcast_to(block[None], (count,) + block.shape)
    gathered = lax.all_to_all(spread, axes, 0, 0, tiled=True)
    return gathered.reshape(total, width)


def _gram_kernel(flats_ref, gram_ref, mean_ref):
    step = pl.program_id(0)

    @pl.when(step == 0)
    def _():
        gram_ref[...] = jnp.zeros_like(gram_ref)

    block = flats_ref[...]
    mean = jnp.sum(block, axis=0) / block.shape[0]
    mean_ref[...] = mean
    total = gram_ref[...]
    for row in range(block.shape[1]):
        centred = block[:, row, :] - mean[row][None, :]
        total += lax.dot_general(
            centred, centred, (((1,), (1,)), ((), ())),
            precision=lax.Precision.HIGHEST, preferred_element_type=jnp.float32,
        )
    gram_ref[...] = total


def frame_gram(flats, width=256):
    frames, rows, cols = flats.shape
    return pl.pallas_call(
        _gram_kernel,
        grid=(cols // width,),
        in_specs=[pl.BlockSpec((frames, rows, width), lambda i: (0, 0, i))],
        out_specs=[
            pl.BlockSpec((frames, frames), lambda i: (0, 0)),
            pl.BlockSpec((rows, width), lambda i: (0, i)),
        ],
        out_shape=[
            jax.ShapeDtypeStruct((frames, frames), jnp.float32),
            jax.ShapeDtypeStruct((rows, cols), jnp.float32),
        ],
    )(flats)


def _project_kernel(lhs_ref, flats_ref, mean_ref, out_ref):
    lhs = lhs_ref[...]
    for row in range(flats_ref.shape[1]):
        centred = flats_ref[:, row, :] - mean_ref[row, :][None, :]
        out_ref[row] = jnp.dot(
            lhs, centred, precision=lax.Precision.HIGH,
            preferred_element_type=jnp.float32,
        )


def project_rows(lhs, flats, mean, block=256):
    m, k = lhs.shape
    _, rows, width = flats.shape
    return pl.pallas_call(
        _project_kernel,
        grid=(width // block,),
        in_specs=[
            pl.BlockSpec((m, k), lambda i: (0, 0)),
            pl.BlockSpec((k, rows, block), lambda i: (0, 0, i)),
            pl.BlockSpec((rows, block), lambda i: (0, i)),
        ],
        out_specs=pl.BlockSpec((rows, m, block), lambda i: (0, 0, i)),
        out_shape=jax.ShapeDtypeStruct((rows, m, width), jnp.float32),
    )(lhs, flats, mean)


def shards(flats, projections, start_basis):
    frames_here, rows_dev, cols_dev = flats.shape
    ang_count = lax.axis_size("ang")
    pix_count = lax.axis_size("pix")
    npix = rows_dev * cols_dev * ang_count * pix_count
    angle_count, rows_all, cols_here = projections.shape

    tiles_in = projections.reshape(angle_count, pix_count, rows_dev, cols_here).transpose(1, 0, 2, 3)
    tiles = lax.all_to_all(tiles_in, "pix", 0, 0, tiled=True)

    local_gram, mean_flat = frame_gram(flats)
    device_count = ang_count * pix_count
    gram_rows = local_gram.reshape(device_count, -1)
    gram = sum_by_exchange(gram_rows, ("ang", "pix"), device_count).reshape(frames_here, frames_here) / npix
    basis = start_basis
    for turn in range(SUBSPACE):
        basis = orthonormal(jnp.dot(gram, basis, precision=lax.Precision.HIGHEST))
    eigen_3d = project_rows(basis.T, flats, mean_flat)
    normal = jnp.dot(
        basis.T,
        jnp.dot(gram, basis, precision=lax.Precision.HIGHEST),
        precision=lax.Precision.HIGHEST,
    )
    eigen_count = basis.shape[1]
    eigen_rows = lax.all_gather(
        eigen_3d, "ang", axis=2, tiled=True
    )
    mean_rows = lax.all_gather(mean_flat, "ang", axis=1, tiled=True)
    eigen_blk = eigen_rows.reshape(rows_dev, eigen_count, pix_count, cols_here)
    mean_blk = mean_rows.reshape(rows_dev, pix_count, cols_here)
    centred_frames = tiles - mean_blk.transpose(1, 0, 2)[:, None]
    partial_value = jnp.einsum(
        "pjrc,rkpc->jk", centred_frames, eigen_blk, precision=lax.Precision.HIGH
    )
    fit_rhs = sum_by_exchange(partial_value, "pix", pix_count) / npix
    weights = solve_normal(normal, fit_rhs)
    estimate = mean_blk.transpose(1, 0, 2)[:, None] + jnp.einsum(
        "jk,rkpc->pjrc", weights, eigen_blk, precision=lax.Precision.HIGH
    )
    tiles_out = tiles / jnp.maximum(estimate, floor_value)
    back = lax.all_to_all(tiles_out, "pix", 0, 0, tiled=True)
    result = back.transpose(1, 0, 2, 3).reshape(angle_count, rows_all, cols_here)
    return result


def solution(mesh):
    in_specs = (P(None, "pix", "ang"), P("ang", None, "pix"), P())
    out_specs = P("ang", None, "pix")
    return jax.shard_map(shards, mesh=mesh, in_specs=in_specs, out_specs=out_specs, check_vma=False)
```

```python
import jax
import jax.numpy as jnp
from jax import lax
from jax.sharding import PartitionSpec as P
from jax.experimental import pallas as pl

SUBSPACE = 2


floor_value = 0.2


def orthonormal(grown):
    correlation = jnp.dot(grown.T, grown, precision=lax.Precision.HIGHEST)
    lower = jnp.linalg.cholesky(correlation)
    return jax.scipy.linalg.solve_triangular(lower, grown.T, lower=True).T


def solve_normal(normal, fit_rhs):
    factor = jnp.linalg.cholesky(normal)
    return jax.scipy.linalg.cho_solve((factor, True), fit_rhs.T).T


def sum_by_exchange(rows, axes, count):
    total, width = rows.shape
    pieces = lax.all_to_all(rows.reshape(count, total // count, width), axes, 0, 0, tiled=True)
    block = jnp.sum(pieces, axis=0)
    spread = jnp.broadcast_to(block[None], (count,) + block.shape)
    gathered = lax.all_to_all(spread, axes, 0, 0, tiled=True)
    return gathered.reshape(total, width)


def _gram_kernel(flats_ref, upper_ref, lower_ref, mean_ref):
    step = pl.program_id(0)

    @pl.when(step == 0)
    def _():
        upper_ref[...] = jnp.zeros_like(upper_ref)
        lower_ref[...] = jnp.zeros_like(lower_ref)

    block = flats_ref[...]
    split = upper_ref.shape[0]
    mean = jnp.sum(block, axis=0) / block.shape[0]
    mean_ref[...] = mean
    upper = upper_ref[...]
    lower = lower_ref[...]
    pair = (((1,), (1,)), ((), ()))
    for row in range(block.shape[1]):
        centred = block[:, row, :] - mean[row][None, :]
        upper += lax.dot_general(
            centred[:split], centred, pair,
            precision=lax.Precision.HIGHEST, preferred_element_type=jnp.float32,
        )
        lower += lax.dot_general(
            centred[split:], centred[split:], pair,
            precision=lax.Precision.HIGHEST, preferred_element_type=jnp.float32,
        )
    upper_ref[...] = upper
    lower_ref[...] = lower


def frame_gram(flats, width=256):
    frames, rows, cols = flats.shape
    split = frames // 2
    upper, lower, mean = pl.pallas_call(
        _gram_kernel,
        grid=(cols // width,),
        in_specs=[pl.BlockSpec((frames, rows, width), lambda i: (0, 0, i))],
        out_specs=[
            pl.BlockSpec((split, frames), lambda i: (0, 0)),
            pl.BlockSpec((frames - split, frames - split), lambda i: (0, 0)),
            pl.BlockSpec((rows, width), lambda i: (0, i)),
        ],
        out_shape=[
            jax.ShapeDtypeStruct((split, frames), jnp.float32),
            jax.ShapeDtypeStruct((frames - split, frames - split), jnp.float32),
            jax.ShapeDtypeStruct((rows, cols), jnp.float32),
        ],
    )(flats)
    below = jnp.concatenate([upper[:, split:].T, lower], axis=1)
    return jnp.concatenate([upper, below], axis=0), mean


def _project_kernel(lhs_ref, flats_ref, mean_ref, out_ref):
    lhs = lhs_ref[...]
    for row in range(flats_ref.shape[1]):
        centred = flats_ref[:, row, :] - mean_ref[row, :][None, :]
        out_ref[row] = jnp.dot(
            lhs, centred, precision=lax.Precision.HIGH,
            preferred_element_type=jnp.float32,
        )


def project_rows(lhs, flats, mean):
    m, k = lhs.shape
    _, rows, width = flats.shape
    return pl.pallas_call(
        _project_kernel,
        grid=(1,),
        in_specs=[
            pl.BlockSpec((m, k), lambda r: (0, 0)),
            pl.BlockSpec((k, rows, width), lambda r: (0, 0, 0)),
            pl.BlockSpec((rows, width), lambda r: (0, 0)),
        ],
        out_specs=pl.BlockSpec((rows, m, width), lambda r: (0, 0, 0)),
        out_shape=jax.ShapeDtypeStruct((rows, m, width), jnp.float32),
    )(lhs, flats, mean)


def shards(flats, projections, start_basis):
    frames_here, rows_dev, cols_dev = flats.shape
    ang_count = lax.axis_size("ang")
    pix_count = lax.axis_size("pix")
    npix = rows_dev * cols_dev * ang_count * pix_count
    angle_count, rows_all, cols_here = projections.shape

    tiles_in = projections.reshape(angle_count, pix_count, rows_dev, cols_here).transpose(1, 0, 2, 3)
    tiles = lax.all_to_all(tiles_in, "pix", 0, 0, tiled=True)

    local_gram, mean_flat = frame_gram(flats)
    device_count = ang_count * pix_count
    gram_rows = local_gram.reshape(device_count, -1)
    gram = sum_by_exchange(gram_rows, ("ang", "pix"), device_count).reshape(frames_here, frames_here) / npix
    basis = start_basis
    for turn in range(SUBSPACE):
        basis = orthonormal(jnp.dot(gram, basis, precision=lax.Precision.HIGHEST))
    eigen_3d = project_rows(basis.T, flats, mean_flat)
    normal = jnp.dot(
        basis.T,
        jnp.dot(gram, basis, precision=lax.Precision.HIGHEST),
        precision=lax.Precision.HIGHEST,
    )
    eigen_count = basis.shape[1]
    eigen_rows = lax.all_gather(
        eigen_3d, "ang", axis=2, tiled=True
    )
    mean_rows = lax.all_gather(mean_flat, "ang", axis=1, tiled=True)
    eigen_blk = eigen_rows.reshape(rows_dev, eigen_count, pix_count, cols_here)
    mean_blk = mean_rows.reshape(rows_dev, pix_count, cols_here)
    centred_frames = tiles - mean_blk.transpose(1, 0, 2)[:, None]
    partial_value = jnp.einsum(
        "pjrc,rkpc->jk", centred_frames, eigen_blk, precision=lax.Precision.HIGH
    )
    fit_rhs = sum_by_exchange(partial_value, "pix", pix_count) / npix
    weights = solve_normal(normal, fit_rhs)
    estimate = mean_blk.transpose(1, 0, 2)[:, None] + jnp.einsum(
        "jk,rkpc->pjrc", weights, eigen_blk, precision=lax.Precision.HIGH
    )
    tiles_out = tiles / jnp.maximum(estimate, floor_value)
    back = lax.all_to_all(tiles_out, "pix", 0, 0, tiled=True)
    result = back.transpose(1, 0, 2, 3).reshape(angle_count, rows_all, cols_here)
    return result


def solution(mesh):
    in_specs = (P(None, "pix", "ang"), P("ang", None, "pix"), P())
    out_specs = P("ang", None, "pix")
    return jax.shard_map(shards, mesh=mesh, in_specs=in_specs, out_specs=out_specs, check_vma=False)
```

```python
import jax
import jax.numpy as jnp
from jax import lax
from jax.sharding import PartitionSpec as P
from jax.experimental import pallas as pl

SUBSPACE = 2


floor_value = 0.2


def orthonormal(grown):
    correlation = jnp.dot(grown.T, grown, precision=lax.Precision.HIGHEST)
    lower = jnp.linalg.cholesky(correlation)
    return jax.scipy.linalg.solve_triangular(lower, grown.T, lower=True).T


def solve_normal(normal, fit_rhs):
    factor = jnp.linalg.cholesky(normal)
    return jax.scipy.linalg.cho_solve((factor, True), fit_rhs.T).T


def sum_by_exchange(rows, axes, count):
    total, width = rows.shape
    pieces = lax.all_to_all(rows.reshape(count, total // count, width), axes, 0, 0, tiled=True)
    block = jnp.sum(pieces, axis=0)
    spread = jnp.broadcast_to(block[None], (count,) + block.shape)
    gathered = lax.all_to_all(spread, axes, 0, 0, tiled=True)
    return gathered.reshape(total, width)


def _gram_kernel(flats_ref, gram_ref, mean_ref):
    step = pl.program_id(0)

    @pl.when(step == 0)
    def _():
        gram_ref[...] = jnp.zeros_like(gram_ref)

    block = flats_ref[...]
    mean = jnp.sum(block, axis=0) / block.shape[0]
    mean_ref[...] = mean
    total = gram_ref[...]
    for row in range(block.shape[1]):
        centred = block[:, row, :] - mean[row][None, :]
        total += lax.dot_general(
            centred, centred, (((1,), (1,)), ((), ())),
            precision=lax.Precision.HIGHEST, preferred_element_type=jnp.float32,
        )
    gram_ref[...] = total


def frame_gram(flats, width=256):
    frames, rows, cols = flats.shape
    return pl.pallas_call(
        _gram_kernel,
        grid=(cols // width,),
        in_specs=[pl.BlockSpec((frames, rows, width), lambda i: (0, 0, i))],
        out_specs=[
            pl.BlockSpec((frames, frames), lambda i: (0, 0)),
            pl.BlockSpec((rows, width), lambda i: (0, i)),
        ],
        out_shape=[
            jax.ShapeDtypeStruct((frames, frames), jnp.float32),
            jax.ShapeDtypeStruct((rows, cols), jnp.float32),
        ],
    )(flats)


def _project_kernel(lhs_ref, flats_ref, mean_ref, out_ref):
    lhs = lhs_ref[...]
    for row in range(flats_ref.shape[1]):
        centred = flats_ref[:, row, :] - mean_ref[row, :][None, :]
        out_ref[row] = jnp.dot(
            lhs, centred, precision=lax.Precision.HIGH,
            preferred_element_type=jnp.float32,
        )


def project_rows(lhs, flats, mean):
    m, k = lhs.shape
    _, rows, width = flats.shape
    return pl.pallas_call(
        _project_kernel,
        grid=(1,),
        in_specs=[
            pl.BlockSpec((m, k), lambda r: (0, 0)),
            pl.BlockSpec((k, rows, width), lambda r: (0, 0, 0)),
            pl.BlockSpec((rows, width), lambda r: (0, 0)),
        ],
        out_specs=pl.BlockSpec((rows, m, width), lambda r: (0, 0, 0)),
        out_shape=jax.ShapeDtypeStruct((rows, m, width), jnp.float32),
    )(lhs, flats, mean)


def shards(flats, projections, start_basis):
    frames_here, rows_dev, cols_dev = flats.shape
    ang_count = lax.axis_size("ang")
    pix_count = lax.axis_size("pix")
    npix = rows_dev * cols_dev * ang_count * pix_count
    angle_count, rows_all, cols_here = projections.shape

    tiles_in = projections.reshape(angle_count, pix_count, rows_dev, cols_here).transpose(1, 0, 2, 3)
    tiles = lax.all_to_all(tiles_in, "pix", 0, 0, tiled=True)

    local_gram, mean_flat = frame_gram(flats)
    device_count = ang_count * pix_count
    gram_rows = local_gram.reshape(device_count, -1)
    gram = sum_by_exchange(gram_rows, ("ang", "pix"), device_count).reshape(frames_here, frames_here) / npix
    basis = start_basis
    for turn in range(SUBSPACE):
        basis = orthonormal(jnp.dot(gram, basis, precision=lax.Precision.HIGHEST))
    eigen_3d = project_rows(basis.T, flats, mean_flat)
    normal = jnp.dot(
        basis.T,
        jnp.dot(gram, basis, precision=lax.Precision.HIGHEST),
        precision=lax.Precision.HIGHEST,
    )
    eigen_count = basis.shape[1]
    eigen_rows = lax.all_gather(
        eigen_3d, "ang", axis=2, tiled=True
    )
    mean_rows = lax.all_gather(mean_flat, "ang", axis=1, tiled=True)
    eigen_blk = eigen_rows.reshape(rows_dev, eigen_count, pix_count, cols_here)
    mean_blk = mean_rows.reshape(rows_dev, pix_count, cols_here)
    centred_frames = tiles - mean_blk.transpose(1, 0, 2)[:, None]
    partial_value = jnp.einsum(
        "pjrc,rkpc->jk", centred_frames, eigen_blk, precision=lax.Precision.HIGH
    )
    fit_rhs = sum_by_exchange(partial_value, "pix", pix_count) / npix
    weights = solve_normal(normal, fit_rhs)
    halves = []
    share = angle_count // 2
    for first in (0, share):
        estimate = mean_blk.transpose(1, 0, 2)[:, None] + jnp.einsum(
            "jk,rkpc->pjrc", weights[first:first + share], eigen_blk, precision=lax.Precision.HIGH
        )
        part = tiles[:, first:first + share] / jnp.maximum(estimate, floor_value)
        back = lax.all_to_all(part, "pix", 0, 0, tiled=True)
        halves.append(back.transpose(1, 0, 2, 3).reshape(share, rows_all, cols_here))
    result = jnp.concatenate(halves, axis=0)
    return result


def solution(mesh):
    in_specs = (P(None, "pix", "ang"), P("ang", None, "pix"), P())
    out_specs = P("ang", None, "pix")
    return jax.shard_map(shards, mesh=mesh, in_specs=in_specs, out_specs=out_specs, check_vma=False)
```

```python
import jax
import jax.numpy as jnp
from jax import lax
from jax.sharding import Mesh, PartitionSpec as P

PIX = ("px", "pz", "pc")
from jax.experimental import pallas as pl

SUBSPACE = 2


floor_value = 0.2


def orthonormal(grown):
    correlation = jnp.dot(grown.T, grown, precision=lax.Precision.HIGHEST)
    lower = jnp.linalg.cholesky(correlation)
    return jax.scipy.linalg.solve_triangular(lower, grown.T, lower=True).T


def solve_normal(normal, fit_rhs):
    factor = jnp.linalg.cholesky(normal)
    return jax.scipy.linalg.cho_solve((factor, True), fit_rhs.T).T


def sum_by_exchange(rows, axes, count):
    total, width = rows.shape
    pieces = lax.all_to_all(rows.reshape(count, total // count, width), axes, 0, 0, tiled=True)
    block = jnp.sum(pieces, axis=0)
    spread = jnp.broadcast_to(block[None], (count,) + block.shape)
    gathered = lax.all_to_all(spread, axes, 0, 0, tiled=True)
    return gathered.reshape(total, width)


def _gram_kernel(flats_ref, gram_ref, mean_ref):
    step = pl.program_id(0)

    @pl.when(step == 0)
    def _():
        gram_ref[...] = jnp.zeros_like(gram_ref)

    block = flats_ref[...]
    mean = jnp.sum(block, axis=0) / block.shape[0]
    mean_ref[...] = mean
    total = gram_ref[...]
    for row in range(block.shape[1]):
        centred = block[:, row, :] - mean[row][None, :]
        total += lax.dot_general(
            centred, centred, (((1,), (1,)), ((), ())),
            precision=lax.Precision.HIGHEST, preferred_element_type=jnp.float32,
        )
    gram_ref[...] = total


def frame_gram(flats, width=256):
    frames, rows, cols = flats.shape
    return pl.pallas_call(
        _gram_kernel,
        grid=(cols // width,),
        in_specs=[pl.BlockSpec((frames, rows, width), lambda i: (0, 0, i))],
        out_specs=[
            pl.BlockSpec((frames, frames), lambda i: (0, 0)),
            pl.BlockSpec((rows, width), lambda i: (0, i)),
        ],
        out_shape=[
            jax.ShapeDtypeStruct((frames, frames), jnp.float32),
            jax.ShapeDtypeStruct((rows, cols), jnp.float32),
        ],
    )(flats)


def _project_kernel(lhs_ref, flats_ref, mean_ref, out_ref):
    lhs = lhs_ref[...]
    for row in range(flats_ref.shape[1]):
        centred = flats_ref[:, row, :] - mean_ref[row, :][None, :]
        out_ref[row] = jnp.dot(
            lhs, centred, precision=lax.Precision.HIGH,
            preferred_element_type=jnp.float32,
        )


def project_rows(lhs, flats, mean):
    m, k = lhs.shape
    _, rows, width = flats.shape
    return pl.pallas_call(
        _project_kernel,
        grid=(1,),
        in_specs=[
            pl.BlockSpec((m, k), lambda r: (0, 0)),
            pl.BlockSpec((k, rows, width), lambda r: (0, 0, 0)),
            pl.BlockSpec((rows, width), lambda r: (0, 0)),
        ],
        out_specs=pl.BlockSpec((rows, m, width), lambda r: (0, 0, 0)),
        out_shape=jax.ShapeDtypeStruct((rows, m, width), jnp.float32),
    )(lhs, flats, mean)


def shards(flats, projections, start_basis):
    frames_here, rows_dev, cols_dev = flats.shape
    ang_count = lax.axis_size("ang")
    pix_count = lax.psum(1, PIX)
    npix = rows_dev * cols_dev * ang_count * pix_count
    angle_count, rows_all, cols_here = projections.shape

    tiles_in = projections.reshape(angle_count, pix_count, rows_dev, cols_here).transpose(1, 0, 2, 3)
    tiles = lax.all_to_all(tiles_in, PIX, 0, 0, tiled=True)

    local_gram, mean_flat = frame_gram(flats)
    device_count = ang_count * pix_count
    gram_rows = local_gram.reshape(device_count, -1)
    gram = sum_by_exchange(gram_rows, ("ang",) + PIX, device_count).reshape(frames_here, frames_here) / npix
    basis = start_basis
    for turn in range(SUBSPACE):
        basis = orthonormal(jnp.dot(gram, basis, precision=lax.Precision.HIGHEST))
    eigen_3d = project_rows(basis.T, flats, mean_flat)
    normal = jnp.dot(
        basis.T,
        jnp.dot(gram, basis, precision=lax.Precision.HIGHEST),
        precision=lax.Precision.HIGHEST,
    )
    eigen_count = basis.shape[1]
    eigen_rows = lax.all_gather(
        eigen_3d, "ang", axis=2, tiled=True
    )
    mean_rows = lax.all_gather(mean_flat, "ang", axis=1, tiled=True)
    eigen_blk = eigen_rows.reshape(rows_dev, eigen_count, pix_count, cols_here)
    mean_blk = mean_rows.reshape(rows_dev, pix_count, cols_here)
    centred_frames = tiles - mean_blk.transpose(1, 0, 2)[:, None]
    partial_value = jnp.einsum(
        "pjrc,rkpc->jk", centred_frames, eigen_blk, precision=lax.Precision.HIGH
    )
    paired = lax.psum(partial_value, PIX[-1])
    fit_rhs = sum_by_exchange(paired, PIX[:-1], pix_count // 2) / npix
    weights = solve_normal(normal, fit_rhs)
    estimate = mean_blk.transpose(1, 0, 2)[:, None] + jnp.einsum(
        "jk,rkpc->pjrc", weights, eigen_blk, precision=lax.Precision.HIGH
    )
    tiles_out = tiles / jnp.maximum(estimate, floor_value)
    back = lax.all_to_all(tiles_out, PIX, 0, 0, tiled=True)
    result = back.transpose(1, 0, 2, 3).reshape(angle_count, rows_all, cols_here)
    return result


def solution(mesh):
    devices = mesh.devices.reshape(mesh.shape["ang"], -1, 4, 2)
    fine = Mesh(devices, ("ang",) + PIX)
    in_specs = (P(None, PIX, "ang"), P("ang", None, PIX), P())
    out_specs = P("ang", None, PIX)
    return jax.shard_map(shards, mesh=fine, in_specs=in_specs, out_specs=out_specs, check_vma=False)
```

```python
import jax
import jax.numpy as jnp
from jax import lax
from jax.sharding import PartitionSpec as P
from jax.experimental import pallas as pl

SUBSPACE = 2


floor_value = 0.2


def orthonormal(grown):
    correlation = jnp.dot(grown.T, grown, precision=lax.Precision.HIGHEST)
    lower = jnp.linalg.cholesky(correlation)
    return jax.scipy.linalg.solve_triangular(lower, grown.T, lower=True).T


def solve_normal(normal, fit_rhs):
    factor = jnp.linalg.cholesky(normal)
    return jax.scipy.linalg.cho_solve((factor, True), fit_rhs.T).T


def sum_by_exchange(rows, axes, count):
    total, width = rows.shape
    pieces = lax.all_to_all(rows.reshape(count, total // count, width), axes, 0, 0, tiled=True)
    block = jnp.sum(pieces, axis=0)
    spread = jnp.broadcast_to(block[None], (count,) + block.shape)
    gathered = lax.all_to_all(spread, axes, 0, 0, tiled=True)
    return gathered.reshape(total, width)


def _gram_kernel(flats_ref, gram_ref, mean_ref):
    step = pl.program_id(0)

    @pl.when(step == 0)
    def _():
        gram_ref[...] = jnp.zeros_like(gram_ref)

    block = flats_ref[...]
    mean = jnp.sum(block, axis=0) / block.shape[0]
    mean_ref[...] = mean
    total = gram_ref[...]
    for row in range(block.shape[1]):
        centred = block[:, row, :] - mean[row][None, :]
        total += lax.dot_general(
            centred, centred, (((1,), (1,)), ((), ())),
            precision=lax.Precision.HIGHEST, preferred_element_type=jnp.float32,
        )
    gram_ref[...] = total


def frame_gram(flats, width=128):
    frames, rows, cols = flats.shape
    return pl.pallas_call(
        _gram_kernel,
        grid=(cols // width,),
        in_specs=[pl.BlockSpec((frames, rows, width), lambda i: (0, 0, i))],
        out_specs=[
            pl.BlockSpec((frames, frames), lambda i: (0, 0)),
            pl.BlockSpec((rows, width), lambda i: (0, i)),
        ],
        out_shape=[
            jax.ShapeDtypeStruct((frames, frames), jnp.float32),
            jax.ShapeDtypeStruct((rows, cols), jnp.float32),
        ],
    )(flats)


def _project_kernel(lhs_ref, flats_ref, mean_ref, out_ref):
    lhs = lhs_ref[...]
    for row in range(flats_ref.shape[1]):
        centred = flats_ref[:, row, :] - mean_ref[row, :][None, :]
        out_ref[row] = jnp.dot(
            lhs, centred, precision=lax.Precision.HIGH,
            preferred_element_type=jnp.float32,
        )


def project_rows(lhs, flats, mean):
    m, k = lhs.shape
    _, rows, width = flats.shape
    return pl.pallas_call(
        _project_kernel,
        grid=(1,),
        in_specs=[
            pl.BlockSpec((m, k), lambda r: (0, 0)),
            pl.BlockSpec((k, rows, width), lambda r: (0, 0, 0)),
            pl.BlockSpec((rows, width), lambda r: (0, 0)),
        ],
        out_specs=pl.BlockSpec((rows, m, width), lambda r: (0, 0, 0)),
        out_shape=jax.ShapeDtypeStruct((rows, m, width), jnp.float32),
    )(lhs, flats, mean)


def shards(flats, projections, start_basis):
    frames_here, rows_dev, cols_dev = flats.shape
    ang_count = lax.axis_size("ang")
    pix_count = lax.axis_size("pix")
    npix = rows_dev * cols_dev * ang_count * pix_count
    angle_count, rows_all, cols_here = projections.shape

    tiles_in = projections.reshape(angle_count, pix_count, rows_dev, cols_here).transpose(1, 0, 2, 3)
    tiles = lax.all_to_all(tiles_in, "pix", 0, 0, tiled=True)

    local_gram, mean_flat = frame_gram(flats)
    device_count = ang_count * pix_count
    gram_rows = local_gram.reshape(device_count, -1)
    gram = sum_by_exchange(gram_rows, ("ang", "pix"), device_count).reshape(frames_here, frames_here) / npix
    basis = start_basis
    for turn in range(SUBSPACE):
        basis = orthonormal(jnp.dot(gram, basis, precision=lax.Precision.HIGHEST))
    eigen_3d = project_rows(basis.T, flats, mean_flat)
    normal = jnp.dot(
        basis.T,
        jnp.dot(gram, basis, precision=lax.Precision.HIGHEST),
        precision=lax.Precision.HIGHEST,
    )
    eigen_count = basis.shape[1]
    eigen_rows = lax.all_gather(
        eigen_3d, "ang", axis=2, tiled=True
    )
    mean_rows = lax.all_gather(mean_flat, "ang", axis=1, tiled=True)
    eigen_blk = eigen_rows.reshape(rows_dev, eigen_count, pix_count, cols_here)
    mean_blk = mean_rows.reshape(rows_dev, pix_count, cols_here)
    centred_frames = tiles - mean_blk.transpose(1, 0, 2)[:, None]
    partial_value = jnp.einsum(
        "pjrc,rkpc->jk", centred_frames, eigen_blk, precision=lax.Precision.HIGH
    )
    fit_rhs = sum_by_exchange(partial_value, "pix", pix_count) / npix
    weights = solve_normal(normal, fit_rhs)
    estimate = mean_blk.transpose(1, 0, 2)[:, None] + jnp.einsum(
        "jk,rkpc->pjrc", weights, eigen_blk, precision=lax.Precision.HIGH
    )
    tiles_out = tiles / jnp.maximum(estimate, floor_value)
    back = lax.all_to_all(tiles_out, "pix", 0, 0, tiled=True)
    result = back.transpose(1, 0, 2, 3).reshape(angle_count, rows_all, cols_here)
    return result


def solution(mesh):
    in_specs = (P(None, "pix", "ang"), P("ang", None, "pix"), P())
    out_specs = P("ang", None, "pix")
    return jax.shard_map(shards, mesh=mesh, in_specs=in_specs, out_specs=out_specs, check_vma=False)
```
